256 devices in a mesh: pipe: 8 (over z_hi, x), expert: 32 (over y, z_lo, core).
Axes of the slice: x: 4, y: 4, z: 8 (z_hi: 2, z_lo: 4; z = z_hi * 4 + z_lo), core: 2. Of those that a mesh axis runs over, the one named last changes fastest.
Arguments:
- grad_out: bfloat16 [8, 4096, 2048], P('pipe', 'expert'), may hold values from -6 to 6
- expert_ids: int32 [8, 4096, 8], P('pipe', 'expert'), may hold values from 0 to 63, as said below
- slot_ids: int32 [8, 4096, 8], P('pipe', 'expert'), may hold values from 0 to 16, as said below
- gate_weights: float32 [8, 4096, 8], P('pipe', 'expert'), may hold values from 0.02 to 0.6
- saved_pre: bfloat16 [8, 64, 512, 1536], P('pipe', 'expert'), may hold values from -6 to 6
- down_weight: bfloat16 [8, 64, 768, 2048], P('pipe', 'expert'), may hold values from -0.21875 to 0.21875
- router_weight: bfloat16 [8, 64, 2048], P('pipe', 'expert'), may hold values from -0.125 to 0.125
Outputs:
- pre_grad: bfloat16 [8, 64, 512, 1536], P('pipe', 'expert')
- grad_inputs: bfloat16 [8, 4096, 2048], P('pipe', 'expert')
The draws below stay inside these ranges and needn't reach their ends.
Inputs may be any that keep to these rules, and one draw needn't show every extreme that they name: `expert_ids`: each row names 8 different experts. `slot_ids`: for the pair (t, k): the number of earlier pairs (by row, then by k) among the same device's 128 rows of that section that name the same expert, capped at 16; the value 16 marks a pair that is dropped.
All inputs are finite; a program needn't handle non-finite values.
Results may differ from the reference program's by a relative error of at most 0.012.
Values may be sent and summed in bfloat16 or wider, within the bound.
No kernel may reach another device: no remote copies, remote signals or barrier semaphores. Data moves between devices by JAX's collectives and lax.ppermute only.
A program may use at most 128 MiB of HBM per device.

```python
import math
import jax
import jax.numpy as jnp
from jax import lax

D = 2048
FF = 768
TOP = 8
TOK_DEV = 128
EXPERTS = 64
TOKENS = 4096
CAP = 16
SLOTS = 512
SECTIONS = 8


def route_tables(key):
    base_key = jax.random.fold_in(key, 11)
    noise_key, level_key, hot_key = jax.random.split(base_key, 3)
    noise = jax.random.randint(noise_key, (SECTIONS, TOKENS, EXPERTS), 0, 2 ** 20)
    levels = jax.random.randint(level_key, (SECTIONS, 1, EXPERTS), 0, 3) * 2 ** 18
    hottest = jax.random.randint(hot_key, (SECTIONS, 1, 1), 0, EXPERTS)
    columns = jnp.arange(EXPERTS, dtype=jnp.int32)
    boost = jnp.where(columns[None, None, :] == hottest, 2 ** 21, 0)
    scores = (noise + levels + boost) * EXPERTS + columns[None, None, :]
    top_values, chosen = lax.top_k(scores.astype(jnp.int32), TOP)
    chosen = chosen.astype(jnp.int32)
    blocks = chosen.reshape(SECTIONS, TOKENS // TOK_DEV, TOK_DEV * TOP)
    onehot = (blocks[..., None] == columns).astype(jnp.int32)
    running = jnp.cumsum(onehot, axis=2)
    ranking = jnp.sum(onehot * running, axis=-1) - 1
    placed = jnp.minimum(ranking, CAP).reshape(SECTIONS, TOKENS, TOP)
    return (chosen, placed.astype(jnp.int32))


def draw_expert_ids(key, part):
    return route_tables(key)[0]


def draw_slot_ids(key, part):
    return route_tables(key)[1]


def level_of(rng, dims, shards, smallest, largest):
    level, own = 1.0, jax.random.fold_in(rng, 6)
    for position, shards_of in shards:
        steps = jnp.exp(jax.random.uniform(jax.random.fold_in(own, position), (shards_of,), jnp.float32, smallest / len(shards), largest / len(shards)))
        level = level * jnp.repeat(steps, dims[position] // shards_of).reshape([-1 if axis == position else 1 for axis in range(len(dims))])
    return level


def bell_draw(own_key, dims, width, bound, shards=(), held_as=jnp.bfloat16):
    drawn = width * jax.random.normal(own_key, dims, jnp.float32)
    if shards:
        drawn = drawn * level_of(own_key, dims, shards, -0.22, 0.18)
    return jnp.clip(drawn, -bound, bound).astype(held_as)


def setup_inputs(seed: int = 0) -> dict:
    keys = jax.random.split(jax.random.key(seed), 8)
    return {
        "grad_out": bell_draw(keys[0], (SECTIONS, TOKENS, D), 1.0, 6.0, ((0, 8), (1, 32))),
        "expert_ids": draw_expert_ids(jax.random.fold_in(keys[7], 71), 0),
        "slot_ids": draw_slot_ids(jax.random.fold_in(keys[7], 71), 0),
        "gate_weights": jnp.clip(jnp.exp(math.log(0.6) - 3.4011974 * jax.random.uniform(keys[3], (SECTIONS, TOKENS, TOP), jnp.float32) ** level_of(keys[3], (SECTIONS, TOKENS, TOP), ((0, 8), (1, 32)), -0.2, 0.2)), 0.02, 0.6),
        "saved_pre": bell_draw(keys[4], (SECTIONS, EXPERTS, SLOTS, 2 * FF), 1.0, 6.0, ((0, 8), (1, 32))),
        "down_weight": bell_draw(keys[5], (SECTIONS, EXPERTS, FF, D), FF ** -0.5, 0.21875, ((0, 8), (1, 32))),
        "router_weight": bell_draw(keys[6], (SECTIONS, EXPERTS, D), D ** -0.5, 0.125, ((0, 8), (1, 32))),
    }


def section_backward(operands):
    grad_out, expert_ids, slot_ids, gate_weights, saved_pre, down_weight, router_weight = operands
    kept_pairs = slot_ids < CAP
    source = (jnp.arange(TOKENS, dtype=jnp.int32) // TOK_DEV)[:, None]
    row_index = expert_ids * SLOTS + source * CAP + jnp.minimum(slot_ids, CAP - 1)
    flat_rows = jnp.where(kept_pairs, row_index, EXPERTS * SLOTS).reshape(-1).astype(jnp.int32)
    gate_low = gate_weights.astype(jnp.bfloat16)
    gate_part = saved_pre[..., :FF].astype(jnp.float32)
    up_part = saved_pre[..., FF:].astype(jnp.float32)
    sigmoid_gate = jax.nn.sigmoid(gate_part)
    silu_gate = gate_part * sigmoid_gate
    hidden = (silu_gate * up_part).astype(jnp.bfloat16)
    weights = down_weight.astype(jnp.float32)
    expert_out = jnp.einsum("esf,efd->esd", hidden.astype(jnp.float32), weights).astype(jnp.bfloat16)
    flat_out = expert_out.reshape(EXPERTS * SLOTS, D)
    pair_out = jnp.take(flat_out, flat_rows, axis=0, mode="fill", fill_value=0)
    features = grad_out.astype(jnp.float32)
    pair_scores = jnp.sum(pair_out.reshape(TOKENS, TOP, D).astype(jnp.float32) * features[:, None, :], axis=-1)
    scaled = (gate_low.astype(jnp.float32)[:, :, None] * features[:, None, :]).astype(jnp.bfloat16)
    scaled_rows = jnp.zeros((EXPERTS * SLOTS, D), jnp.bfloat16).at[flat_rows].set(scaled.reshape(TOKENS * TOP, D), mode="drop")
    scaled_rows = scaled_rows.reshape(EXPERTS, SLOTS, D)
    row_grad = jnp.einsum("esd,efd->esf", scaled_rows.astype(jnp.float32), weights)
    gate_grad = row_grad * up_part * sigmoid_gate * (1.0 + gate_part * (1.0 - sigmoid_gate))
    up_grad = row_grad * silu_gate
    pre_grad = jnp.concatenate([gate_grad, up_grad], axis=-1).astype(jnp.bfloat16)
    weighted_sum = jnp.sum(gate_weights * pair_scores, axis=-1, keepdims=True)
    select_grad = gate_weights * (pair_scores - weighted_sum)
    columns = jnp.arange(EXPERTS, dtype=jnp.int32)
    matches = expert_ids[:, :, None] == columns[None, None, :]
    logit_grad = jnp.sum(jnp.where(matches, select_grad[:, :, None], jnp.float32(0.0)), axis=1).astype(jnp.bfloat16)
    router_part = jnp.dot(logit_grad, router_weight, preferred_element_type=jnp.float32)
    section_grad = (features + router_part).astype(jnp.bfloat16)
    return pre_grad, section_grad


def reference(grad_out, expert_ids, slot_ids, gate_weights, saved_pre, down_weight, router_weight):
    pre_grad, section_grad = lax.map(section_backward, (grad_out, expert_ids, slot_ids, gate_weights, saved_pre, down_weight, router_weight))
    grad_inputs = jnp.roll(section_grad, -1, axis=0)
    return pre_grad, grad_inputs
```

```python
import jax
import jax.numpy as jnp
from jax import lax
from jax.sharding import PartitionSpec as P


def passed_along(value, axis, by):
    peers = lax.axis_size(axis)
    return lax.ppermute(value, axis, [(i, (i + by) % peers) for i in range(peers)])


def per_device(grad_out, expert_ids, slot_ids, gate_weights, saved_pre, down_weight, router_weight):
    groups = lax.axis_size("expert")
    local_experts = down_weight.shape[1]
    hidden_width = down_weight.shape[2]
    tok_rows = grad_out.shape[1]
    width = grad_out.shape[2]
    top_count = expert_ids.shape[2]
    expert_total = local_experts * groups
    capacity = tok_rows * top_count // expert_total
    total_rows = expert_total * capacity
    features = grad_out[0]
    route_ids = expert_ids[0]
    kept_pairs = slot_ids[0] < capacity
    destination = (
        route_ids % local_experts * (groups * capacity)
        + route_ids // local_experts * capacity
        + jnp.minimum(slot_ids[0], capacity - 1)
    )
    pair_dest = jnp.where(kept_pairs, destination, total_rows).reshape(-1)
    row_ids = jnp.arange(total_rows, dtype=jnp.int32)
    matches = pair_dest[None, :] == row_ids[:, None]
    pair_token = jnp.arange(tok_rows * top_count, dtype=jnp.int32) // top_count
    slot_token = jnp.sum(jnp.where(matches, pair_token[None, :], 0), axis=1)
    occupied = jnp.any(matches, axis=1)
    gate_low = gate_weights[0].astype(jnp.bfloat16)
    slot_gate = jnp.sum(
        jnp.where(matches, gate_low.reshape(-1).astype(jnp.float32)[None, :], jnp.float32(0.0)),
        axis=1,
    )
    token_rows = jnp.take(features, slot_token, axis=0)
    token_rows = jnp.where(occupied[:, None], token_rows, jnp.zeros_like(token_rows))

    gate_out = (
        slot_gate.reshape(local_experts, groups, capacity)
        .transpose(1, 0, 2)
        .reshape(groups, local_experts * capacity)
        .astype(jnp.bfloat16)
    )
    router_out = jnp.broadcast_to(
        router_weight[0].reshape(1, local_experts * width), (groups, local_experts * width)
    )
    small = jnp.concatenate([gate_out, router_out], axis=1)
    small_in = lax.all_to_all(small, "expert", split_axis=0, concat_axis=0, tiled=True)
    gate_in = (
        small_in[:, : local_experts * capacity]
        .reshape(groups, local_experts, capacity)
        .transpose(1, 0, 2)
        .reshape(local_experts, groups * capacity)
        .astype(jnp.float32)
    )
    router_full = small_in[:, local_experts * capacity :].reshape(expert_total, width)

    arrived = lax.all_to_all(
        token_rows.reshape(local_experts, groups, capacity, -1),
        "expert",
        split_axis=1,
        concat_axis=1,
        tiled=True,
    )
    rows_in = arrived.reshape(local_experts, groups * capacity, -1).astype(jnp.float32)

    pre_saved = saved_pre[0]
    gate_part = pre_saved[..., :hidden_width].astype(jnp.float32)
    up_part = pre_saved[..., hidden_width:].astype(jnp.float32)
    sigmoid_gate = jax.nn.sigmoid(gate_part)
    silu_gate = gate_part * sigmoid_gate
    hidden = (silu_gate * up_part).astype(jnp.bfloat16)
    weights = down_weight[0]
    expert_out = jnp.einsum(
        "jsf,jfd->jsd", hidden, weights, preferred_element_type=jnp.float32
    ).astype(jnp.bfloat16)
    row_scores = jnp.sum(rows_in * lax.optimization_barrier(expert_out).astype(jnp.float32), axis=-1)
    returned = lax.all_to_all(
        row_scores.reshape(local_experts, groups, capacity),
        "expert",
        split_axis=1,
        concat_axis=1,
        tiled=True,
    )
    pair_scores = jnp.take(
        returned.reshape(total_rows), pair_dest, axis=0, mode="fill", fill_value=0
    ).reshape(tok_rows, top_count)

    scaled_rows = (gate_in[..., None] * rows_in).astype(jnp.bfloat16)
    row_grad = jnp.einsum("jsd,jfd->jsf", scaled_rows, weights, preferred_element_type=jnp.float32)
    gate_grad = row_grad * up_part * sigmoid_gate * (1.0 + gate_part * (1.0 - sigmoid_gate))
    up_grad = row_grad * silu_gate
    pre_grad = jnp.concatenate([gate_grad, up_grad], axis=-1).astype(jnp.bfloat16)

    gate_values = gate_weights[0]
    weighted_sum = jnp.sum(gate_values * pair_scores, axis=-1, keepdims=True)
    select_grad = gate_values * (pair_scores - weighted_sum)
    expert_columns = jnp.arange(expert_total, dtype=jnp.int32)
    chosen = route_ids[:, :, None] == expert_columns[None, None, :]
    logit_grad = jnp.sum(
        jnp.where(chosen, select_grad[:, :, None], jnp.float32(0.0)), axis=1
    ).astype(jnp.bfloat16)
    router_part = jnp.dot(logit_grad, router_full, preferred_element_type=jnp.float32)
    section_grad = (features.astype(jnp.float32) + router_part).astype(jnp.bfloat16)
    outgoing = passed_along(section_grad, "pipe", -1)
    return (pre_grad[None], outgoing[None])


def solution(mesh):
    in_specs = (
        P("pipe", "expert", None),
        P("pipe", "expert", None),
        P("pipe", "expert", None),
        P("pipe", "expert", None),
        P("pipe", "expert", None, None),
        P("pipe", "expert", None, None),
        P("pipe", "expert", None),
    )
    out_specs = (P("pipe", "expert", None, None), P("pipe", "expert", None))
    return jax.shard_map(
        per_device, mesh=mesh, in_specs=in_specs, out_specs=out_specs, check_vma=False
    )
```

```python
import jax
import jax.numpy as jnp
from jax import lax
from jax.sharding import PartitionSpec as P


def passed_along(value, axis, by):
    peers = lax.axis_size(axis)
    return lax.ppermute(value, axis, [(i, (i + by) % peers) for i in range(peers)])


def per_device(grad_out, expert_ids, slot_ids, gate_weights, saved_pre, down_weight, router_weight):
    groups = lax.axis_size("expert")
    local_experts = down_weight.shape[1]
    hidden_width = down_weight.shape[2]
    tok_rows = grad_out.shape[1]
    width = grad_out.shape[2]
    top_count = expert_ids.shape[2]
    expert_total = local_experts * groups
    capacity = tok_rows * top_count // expert_total
    total_rows = expert_total * capacity
    features = grad_out[0]

    next_features = passed_along(features, "pipe", -1)
    next_router = passed_along(router_weight[0], "pipe", -1)

    route_ids = expert_ids[0]
    kept_pairs = slot_ids[0] < capacity
    destination = (
        route_ids % local_experts * (groups * capacity)
        + route_ids // local_experts * capacity
        + jnp.minimum(slot_ids[0], capacity - 1)
    )
    pair_dest = jnp.where(kept_pairs, destination, total_rows)
    row_ids = jnp.arange(total_rows, dtype=jnp.int32)
    token_hit = pair_dest[None, :, :] == row_ids[:, None, None]
    token_onehot = jnp.any(token_hit, axis=2).astype(jnp.bfloat16)
    token_rows = jnp.dot(token_onehot, features, preferred_element_type=jnp.float32).astype(jnp.bfloat16)
    matches = token_hit.reshape(total_rows, tok_rows * top_count)
    gate_low = gate_weights[0].astype(jnp.bfloat16)
    slot_gate = jnp.sum(
        jnp.where(matches, gate_low.reshape(-1).astype(jnp.float32)[None, :], jnp.float32(0.0)),
        axis=1,
    )

    arrived = lax.all_to_all(
        token_rows.reshape(local_experts, groups, capacity, -1),
        "expert",
        split_axis=1,
        concat_axis=1,
        tiled=True,
    )

    me = lax.axis_index("expert")
    gate_table = (
        slot_gate.reshape(local_experts, groups, capacity)
        .transpose(1, 0, 2)
        .reshape(1, total_rows)
        .astype(jnp.bfloat16)
    )
    own_block = jnp.concatenate([gate_table, next_router.reshape(1, local_experts * width)], axis=1)
    blocks = lax.dynamic_update_slice(
        jnp.zeros((groups, own_block.shape[1]), jnp.bfloat16), own_block, (me, 0)
    )
    gathered = lax.psum(blocks, "expert")
    gate_in = (
        lax.dynamic_slice_in_dim(gathered[:, :total_rows], me * local_experts * capacity, local_experts * capacity, axis=1)
        .reshape(groups, local_experts, capacity)
        .transpose(1, 0, 2)
        .reshape(local_experts, groups * capacity)
        .astype(jnp.float32)
    )
    next_router_full = gathered[:, total_rows:].reshape(expert_total, width)

    rows_in = arrived.reshape(local_experts, groups * capacity, -1).astype(jnp.float32)

    pre_saved = saved_pre[0]
    gate_part = pre_saved[..., :hidden_width].astype(jnp.float32)
    up_part = pre_saved[..., hidden_width:].astype(jnp.float32)
    sigmoid_gate = jax.nn.sigmoid(gate_part)
    silu_gate = gate_part * sigmoid_gate
    hidden = (silu_gate * up_part).astype(jnp.bfloat16)
    weights = down_weight[0]
    expert_out = jnp.einsum(
        "jsf,jfd->jsd", hidden, weights, preferred_element_type=jnp.float32
    ).astype(jnp.bfloat16)
    row_scores = jnp.sum(rows_in * lax.optimization_barrier(expert_out).astype(jnp.float32), axis=-1)
    returned = lax.all_to_all(
        row_scores.reshape(local_experts, groups, capacity),
        "expert",
        split_axis=1,
        concat_axis=1,
        tiled=True,
    )
    pair_scores = jnp.sum(
        jnp.where(matches, returned.reshape(total_rows)[:, None], jnp.float32(0.0)), axis=0
    ).reshape(tok_rows, top_count)

    scaled_rows = (gate_in[..., None] * rows_in).astype(jnp.bfloat16)
    row_grad = jnp.einsum("jsd,jfd->jsf", scaled_rows, weights, preferred_element_type=jnp.float32)
    gate_grad = row_grad * up_part * sigmoid_gate * (1.0 + gate_part * (1.0 - sigmoid_gate))
    up_grad = row_grad * silu_gate
    pre_grad = jnp.concatenate([gate_grad, up_grad], axis=-1).astype(jnp.bfloat16)

    gate_values = gate_weights[0]
    weighted_sum = jnp.sum(gate_values * pair_scores, axis=-1, keepdims=True)
    select_grad = gate_values * (pair_scores - weighted_sum)
    expert_columns = jnp.arange(expert_total, dtype=jnp.int32)
    chosen = route_ids[:, :, None] == expert_columns[None, None, :]
    logit_grad = jnp.sum(
        jnp.where(chosen, select_grad[:, :, None], jnp.float32(0.0)), axis=1
    ).astype(jnp.bfloat16)
    next_logit_grad = passed_along(logit_grad, "pipe", -1)
    router_part = jnp.dot(next_logit_grad, next_router_full, preferred_element_type=jnp.float32)
    outgoing = (next_features.astype(jnp.float32) + router_part).astype(jnp.bfloat16)
    return (pre_grad[None], outgoing[None])


def solution(mesh):
    in_specs = (
        P("pipe", "expert", None),
        P("pipe", "expert", None),
        P("pipe", "expert", None),
        P("pipe", "expert", None),
        P("pipe", "expert", None, None),
        P("pipe", "expert", None, None),
        P("pipe", "expert", None),
    )
    out_specs = (P("pipe", "expert", None, None), P("pipe", "expert", None))
    return jax.shard_map(
        per_device, mesh=mesh, in_specs=in_specs, out_specs=out_specs, check_vma=False
    )
```

```python
import jax
import jax.numpy as jnp
from jax import lax
from jax.sharding import PartitionSpec as P


def passed_along(value, axis, by):
    peers = lax.axis_size(axis)
    return lax.ppermute(value, axis, [(i, (i + by) % peers) for i in range(peers)])


def per_device(grad_out, expert_ids, slot_ids, gate_weights, saved_pre, down_weight, router_weight):
    groups = lax.axis_size("expert")
    local_experts = down_weight.shape[1]
    hidden_width = down_weight.shape[2]
    tok_rows = grad_out.shape[1]
    width = grad_out.shape[2]
    top_count = expert_ids.shape[2]
    expert_total = local_experts * groups
    capacity = tok_rows * top_count // expert_total
    total_rows = expert_total * capacity
    chunk = width // capacity
    features = grad_out[0]

    route_ids = expert_ids[0]
    kept_pairs = slot_ids[0] < capacity
    destination = (
        route_ids % local_experts * (groups * capacity)
        + route_ids // local_experts * capacity
        + jnp.minimum(slot_ids[0], capacity - 1)
    )
    pair_dest = jnp.where(kept_pairs, destination, total_rows)
    row_ids = jnp.arange(total_rows, dtype=jnp.int32)
    token_hit = pair_dest[None, :, :] == row_ids[:, None, None]
    token_onehot = jnp.any(token_hit, axis=2).astype(jnp.bfloat16)
    token_rows = jnp.dot(token_onehot, features, preferred_element_type=jnp.float32).astype(jnp.bfloat16)
    matches = token_hit.reshape(total_rows, tok_rows * top_count)
    gate_low = gate_weights[0].astype(jnp.bfloat16)
    slot_gate = jnp.sum(
        jnp.where(matches, gate_low.reshape(-1).astype(jnp.float32)[None, :], jnp.float32(0.0)),
        axis=1,
    )

    gate_cols = jnp.zeros((total_rows, 128), jnp.bfloat16).at[:, 0].set(slot_gate.astype(jnp.bfloat16))
    router_chunks = jnp.broadcast_to(
        router_weight[0].reshape(local_experts, 1, capacity, chunk),
        (local_experts, groups, capacity, chunk),
    ).reshape(total_rows, chunk)
    payload = jnp.concatenate([token_rows, router_chunks, gate_cols], axis=1)
    arrived = lax.all_to_all(
        payload.reshape(local_experts, groups, capacity, -1),
        "expert",
        split_axis=1,
        concat_axis=1,
        tiled=True,
    )
    gate_in = arrived[..., width + chunk].reshape(local_experts, groups * capacity).astype(jnp.float32)
    router_full = arrived[..., width : width + chunk].transpose(1, 0, 2, 3).reshape(expert_total, width)
    rows_in = arrived[..., :width].reshape(local_experts, groups * capacity, width).astype(jnp.float32)

    pre_saved = saved_pre[0]
    gate_part = pre_saved[..., :hidden_width].astype(jnp.float32)
    up_part = pre_saved[..., hidden_width:].astype(jnp.float32)
    sigmoid_gate = jax.nn.sigmoid(gate_part)
    silu_gate = gate_part * sigmoid_gate
    hidden = (silu_gate * up_part).astype(jnp.bfloat16)
    weights = down_weight[0]
    expert_out = jnp.einsum(
        "jsf,jfd->jsd", hidden, weights, preferred_element_type=jnp.float32
    ).astype(jnp.bfloat16)
    row_scores = jnp.sum(rows_in * lax.optimization_barrier(expert_out).astype(jnp.float32), axis=-1)
    returned = lax.all_to_all(
        row_scores.reshape(local_experts, groups, capacity),
        "expert",
        split_axis=1,
        concat_axis=1,
        tiled=True,
    )
    pair_scores = jnp.sum(
        jnp.where(matches, returned.reshape(total_rows)[:, None], jnp.float32(0.0)), axis=0
    ).reshape(tok_rows, top_count)

    scaled_rows = (gate_in[..., None] * rows_in).astype(jnp.bfloat16)
    row_grad = jnp.einsum("jsd,jfd->jsf", scaled_rows, weights, preferred_element_type=jnp.float32)
    gate_grad = row_grad * up_part * sigmoid_gate * (1.0 + gate_part * (1.0 - sigmoid_gate))
    up_grad = row_grad * silu_gate
    pre_grad = jnp.concatenate([gate_grad, up_grad], axis=-1).astype(jnp.bfloat16)

    gate_values = gate_weights[0]
    weighted_sum = jnp.sum(gate_values * pair_scores, axis=-1, keepdims=True)
    select_grad = gate_values * (pair_scores - weighted_sum)
    expert_columns = jnp.arange(expert_total, dtype=jnp.int32)
    chosen = route_ids[:, :, None] == expert_columns[None, None, :]
    logit_grad = jnp.sum(
        jnp.where(chosen, select_grad[:, :, None], jnp.float32(0.0)), axis=1
    ).astype(jnp.bfloat16)
    router_part = jnp.dot(logit_grad, router_full, preferred_element_type=jnp.float32)
    section_grad = (features.astype(jnp.float32) + router_part).astype(jnp.bfloat16)
    outgoing = passed_along(section_grad, "pipe", -1)
    return (pre_grad[None], outgoing[None])


def solution(mesh):
    in_specs = (
        P("pipe", "expert", None),
        P("pipe", "expert", None),
        P("pipe", "expert", None),
        P("pipe", "expert", None),
        P("pipe", "expert", None, None),
        P("pipe", "expert", None, None),
        P("pipe", "expert", None),
    )
    out_specs = (P("pipe", "expert", None, None), P("pipe", "expert", None))
    return jax.shard_map(
        per_device, mesh=mesh, in_specs=in_specs, out_specs=out_specs, check_vma=False
    )
```

```python
import jax
import jax.numpy as jnp
import numpy as np
from jax import lax
from jax.sharding import Mesh, PartitionSpec as P

EXPERT_AXES = ("y", "zl", "core")
RING_AXES = ("y", "core")


def passed_along(value, axis, by):
    peers = lax.axis_size(axis)
    return lax.ppermute(value, axis, [(i, (i + by) % peers) for i in range(peers)])


def per_device(grad_out, expert_ids, slot_ids, gate_weights, saved_pre, down_weight, router_weight):
    ring_y = lax.axis_size("y")
    ring_z = lax.axis_size("zl")
    ring_c = lax.axis_size("core")
    groups = ring_y * ring_z * ring_c
    ring = ring_y * ring_c
    local_experts = down_weight.shape[1]
    hidden_width = down_weight.shape[2]
    tok_rows = grad_out.shape[1]
    width = grad_out.shape[2]
    top_count = expert_ids.shape[2]
    expert_total = local_experts * groups
    capacity = tok_rows * top_count // expert_total
    total_rows = expert_total * capacity
    features = grad_out[0]
    my_z = lax.axis_index("zl")

    route_ids = expert_ids[0]
    kept_pairs = slot_ids[0] < capacity
    destination = (
        route_ids % local_experts * (groups * capacity)
        + route_ids // local_experts * capacity
        + jnp.minimum(slot_ids[0], capacity - 1)
    )
    pair_dest = jnp.where(kept_pairs, destination, total_rows)
    row_ids = jnp.arange(total_rows, dtype=jnp.int32)
    matches = (pair_dest[None, :, :] == row_ids[:, None, None]).reshape(total_rows, tok_rows * top_count)

    router_flat = router_weight[0].reshape(tok_rows, local_experts * width // tok_rows)
    extras = jnp.concatenate(
        [
            route_ids.astype(jnp.bfloat16),
            slot_ids[0].astype(jnp.bfloat16),
            gate_weights[0].astype(jnp.bfloat16),
            jnp.zeros((tok_rows, 32 - 3 * top_count), jnp.bfloat16),
            router_flat,
            jnp.zeros((tok_rows, 128 - 32 - router_flat.shape[1]), jnp.bfloat16),
        ],
        axis=1,
    )
    own = jnp.concatenate([features, extras], axis=1)
    stage_a = lax.all_to_all(
        jnp.broadcast_to(own[None], (ring_z,) + own.shape), "zl", split_axis=0, concat_axis=0, tiled=True
    )
    near_rows = stage_a[..., :width].reshape(ring_z * tok_rows, width)
    near_ids = stage_a[..., width : width + top_count].astype(jnp.int32)
    near_slots = stage_a[..., width + top_count : width + 2 * top_count].astype(jnp.int32)
    near_gates = stage_a[..., width + 2 * top_count : width + 3 * top_count].astype(jnp.float32)
    near_router = stage_a[..., width + 32 : width + 32 + router_flat.shape[1]].reshape(
        ring_z, local_experts, width
    )

    dev = near_ids // local_experts
    dest_y = dev // (ring_z * ring_c)
    dest_z = dev // ring_c % ring_z
    dest_c = dev % ring_c
    dest_j = near_ids % local_experts
    source_z = jnp.arange(ring_z, dtype=jnp.int32)[:, None, None]
    ring_rows = ring * local_experts * ring_z * capacity
    near_dest = (
        ((dest_y * ring_c + dest_c) * local_experts + dest_j) * ring_z + source_z
    ) * capacity + jnp.minimum(near_slots, capacity - 1)
    near_dest = jnp.where((near_slots < capacity) & (dest_z == my_z), near_dest, ring_rows)
    ring_ids = jnp.arange(ring_rows, dtype=jnp.int32)
    near_hit = near_dest.reshape(ring_z * tok_rows, top_count)[None, :, :] == ring_ids[:, None, None]
    near_onehot = jnp.any(near_hit, axis=2).astype(jnp.bfloat16)
    ring_tokens = jnp.dot(near_onehot, near_rows, preferred_element_type=jnp.float32).astype(jnp.bfloat16)
    ring_gate = jnp.sum(
        jnp.where(near_hit, near_gates.reshape(ring_z * tok_rows, top_count)[None], jnp.float32(0.0)),
        axis=(1, 2),
    )
    rows_per_dest = local_experts * ring_z * capacity
    router_cols = jnp.broadcast_to(
        near_router.reshape(1, rows_per_dest, ring_z * local_experts * width // rows_per_dest),
        (ring, rows_per_dest, ring_z * local_experts * width // rows_per_dest),
    ).reshape(ring_rows, -1)
    gate_cols = jnp.zeros((ring_rows, 128), jnp.bfloat16).at[:, 0].set(ring_gate.astype(jnp.bfloat16))
    payload = jnp.concatenate([ring_tokens, router_cols, gate_cols], axis=1)
    arrived = lax.all_to_all(
        payload.reshape(ring, rows_per_dest, -1), RING_AXES, split_axis=0, concat_axis=0, tiled=True
    ).reshape(ring_y, ring_c, local_experts, ring_z, capacity, -1)
    arrived_rows = arrived.transpose(2, 0, 3, 1, 4, 5).reshape(local_experts, groups * capacity, -1)
    rows_in = arrived_rows[..., :width].astype(jnp.float32)
    router_w = router_cols.shape[1]
    gate_in = arrived_rows[..., width + router_w].astype(jnp.float32)
    router_full = (
        arrived[:, :, :, :, :, width : width + router_w]
        .reshape(ring_y, ring_c, ring_z, local_experts, width)
        .transpose(0, 2, 1, 3, 4)
        .reshape(expert_total, width)
    )

    pre_saved = saved_pre[0]
    gate_part = pre_saved[..., :hidden_width].astype(jnp.float32)
    up_part = pre_saved[..., hidden_width:].astype(jnp.float32)
    sigmoid_gate = jax.nn.sigmoid(gate_part)
    silu_gate = gate_part * sigmoid_gate
    hidden = (silu_gate * up_part).astype(jnp.bfloat16)
    weights = down_weight[0]
    expert_out = jnp.einsum(
        "jsf,jfd->jsd", hidden, weights, preferred_element_type=jnp.float32
    ).astype(jnp.bfloat16)
    row_scores = jnp.sum(rows_in * lax.optimization_barrier(expert_out).astype(jnp.float32), axis=-1)
    returned = lax.all_to_all(
        row_scores.reshape(local_experts, groups, capacity),
        EXPERT_AXES,
        split_axis=1,
        concat_axis=1,
        tiled=True,
    )
    pair_scores = jnp.sum(
        jnp.where(matches, returned.reshape(total_rows)[:, None], jnp.float32(0.0)), axis=0
    ).reshape(tok_rows, top_count)

    scaled_rows = (gate_in[..., None] * rows_in).astype(jnp.bfloat16)
    row_grad = jnp.einsum("jsd,jfd->jsf", scaled_rows, weights, preferred_element_type=jnp.float32)
    gate_grad = row_grad * up_part * sigmoid_gate * (1.0 + gate_part * (1.0 - sigmoid_gate))
    up_grad = row_grad * silu_gate
    pre_grad = jnp.concatenate([gate_grad, up_grad], axis=-1).astype(jnp.bfloat16)

    gate_values = gate_weights[0]
    weighted_sum = jnp.sum(gate_values * pair_scores, axis=-1, keepdims=True)
    select_grad = gate_values * (pair_scores - weighted_sum)
    expert_columns = jnp.arange(expert_total, dtype=jnp.int32)
    chosen = route_ids[:, :, None] == expert_columns[None, None, :]
    logit_grad = jnp.sum(
        jnp.where(chosen, select_grad[:, :, None], jnp.float32(0.0)), axis=1
    ).astype(jnp.bfloat16)
    router_part = jnp.dot(logit_grad, router_full, preferred_element_type=jnp.float32)
    section_grad = (features.astype(jnp.float32) + router_part).astype(jnp.bfloat16)
    outgoing = passed_along(section_grad, "pipe", -1)
    return (pre_grad[None], outgoing[None])


def ring_shape(mesh):
    row = mesh.devices[0]
    try:
        ys = sorted({d.coords[1] for d in row})
        zs = sorted({d.coords[2] for d in row})
        cs = sorted({d.core_on_chip for d in row})
        return len(ys), len(zs), len(cs)
    except AttributeError:
        return 4, row.size // 8, 2


def solution(mesh):
    ring_y, ring_z, ring_c = ring_shape(mesh)
    fine = Mesh(
        np.asarray(mesh.devices).reshape(mesh.devices.shape[0], ring_y, ring_z, ring_c),
        ("pipe",) + EXPERT_AXES,
    )
    in_specs = (
        P("pipe", EXPERT_AXES, None),
        P("pipe", EXPERT_AXES, None),
        P("pipe", EXPERT_AXES, None),
        P("pipe", EXPERT_AXES, None),
        P("pipe", EXPERT_AXES, None, None),
        P("pipe", EXPERT_AXES, None, None),
        P("pipe", EXPERT_AXES, None),
    )
    out_specs = (P("pipe", EXPERT_AXES, None, None), P("pipe", EXPERT_AXES, None))
    return jax.shard_map(
        per_device, mesh=fine, in_specs=in_specs, out_specs=out_specs, check_vma=False
    )
```

```python
import jax
import jax.numpy as jnp
from jax import lax
from jax.sharding import PartitionSpec as P


def passed_along(value, axis, by):
    peers = lax.axis_size(axis)
    return lax.ppermute(value, axis, [(i, (i + by) % peers) for i in range(peers)])


def per_device(grad_out, expert_ids, slot_ids, gate_weights, saved_pre, down_weight, router_weight):
    groups = lax.axis_size("expert")
    local_experts = down_weight.shape[1]
    hidden_width = down_weight.shape[2]
    tok_rows = grad_out.shape[1]
    width = grad_out.shape[2]
    top_count = expert_ids.shape[2]
    expert_total = local_experts * groups
    capacity = tok_rows * top_count // expert_total
    total_rows = expert_total * capacity
    chunk = width // capacity
    features = grad_out[0]

    route_ids = expert_ids[0]
    kept_pairs = slot_ids[0] < capacity
    pair_dest = jnp.where(kept_pairs, route_ids * capacity + jnp.minimum(slot_ids[0], capacity - 1), total_rows)
    row_ids = jnp.arange(total_rows, dtype=jnp.int32)
    token_hit = pair_dest[None, :, :] == row_ids[:, None, None]
    token_onehot = jnp.any(token_hit, axis=2).astype(jnp.bfloat16)
    token_rows = jnp.dot(token_onehot, features, preferred_element_type=jnp.float32).astype(jnp.bfloat16)
    matches = token_hit.reshape(total_rows, tok_rows * top_count)
    gate_low = gate_weights[0].astype(jnp.bfloat16)
    slot_gate = jnp.sum(
        jnp.where(matches, gate_low.reshape(-1).astype(jnp.float32)[None, :], jnp.float32(0.0)),
        axis=1,
    )

    gate_cols = jnp.zeros((total_rows, 128), jnp.bfloat16).at[:, 0].set(slot_gate.astype(jnp.bfloat16))
    router_chunks = jnp.broadcast_to(
        router_weight[0].reshape(1, local_experts * capacity, chunk),
        (groups, local_experts * capacity, chunk),
    ).reshape(total_rows, chunk)
    payload = jnp.concatenate([token_rows, router_chunks, gate_cols], axis=1)
    arrived = lax.all_to_all(
        payload.reshape(groups, local_experts * capacity, -1),
        "expert",
        split_axis=0,
        concat_axis=0,
        tiled=True,
    )
    gate_in = arrived[..., width + chunk].reshape(groups, local_experts, capacity).astype(jnp.float32)
    router_full = arrived[..., width : width + chunk].reshape(expert_total, width)
    rows_in = arrived[..., :width].reshape(groups, local_experts, capacity, width).astype(jnp.float32)

    next_pack = passed_along(jnp.concatenate([features, router_full], axis=0), "pipe", -1)

    pre_saved = saved_pre[0]
    gate_part = pre_saved[..., :hidden_width].astype(jnp.float32)
    up_part = pre_saved[..., hidden_width:].astype(jnp.float32)
    sigmoid_gate = jax.nn.sigmoid(gate_part)
    silu_gate = gate_part * sigmoid_gate
    hidden = (silu_gate * up_part).astype(jnp.bfloat16)
    weights = down_weight[0]
    expert_out = jnp.einsum(
        "jsf,jfd->jsd", hidden, weights, preferred_element_type=jnp.float32
    ).astype(jnp.bfloat16)
    expert_out = lax.optimization_barrier(expert_out).reshape(local_experts, groups, capacity, width)
    row_scores = jnp.sum(
        rows_in * expert_out.transpose(1, 0, 2, 3).astype(jnp.float32), axis=-1
    )
    returned = lax.all_to_all(
        row_scores.reshape(groups, local_experts * capacity),
        "expert",
        split_axis=0,
        concat_axis=0,
        tiled=True,
    )
    pair_scores = jnp.sum(
        jnp.where(matches, returned.reshape(total_rows)[:, None], jnp.float32(0.0)), axis=0
    ).reshape(tok_rows, top_count)

    scaled_rows = (gate_in[..., None] * rows_in).astype(jnp.bfloat16)
    row_grad = jnp.einsum(
        "gjsd,jfd->jgsf", scaled_rows, weights, preferred_element_type=jnp.float32
    ).reshape(local_experts, groups * capacity, hidden_width)
    gate_grad = row_grad * up_part * sigmoid_gate * (1.0 + gate_part * (1.0 - sigmoid_gate))
    up_grad = row_grad * silu_gate
    pre_grad = jnp.concatenate([gate_grad, up_grad], axis=-1).astype(jnp.bfloat16)

    gate_values = gate_weights[0]
    weighted_sum = jnp.sum(gate_values * pair_scores, axis=-1, keepdims=True)
    select_grad = gate_values * (pair_scores - weighted_sum)
    expert_columns = jnp.arange(expert_total, dtype=jnp.int32)
    chosen = route_ids[:, :, None] == expert_columns[None, None, :]
    logit_grad = jnp.sum(
        jnp.where(chosen, select_grad[:, :, None], jnp.float32(0.0)), axis=1
    ).astype(jnp.bfloat16)
    next_logit_grad = passed_along(logit_grad, "pipe", -1)
    router_part = jnp.dot(next_logit_grad, next_pack[tok_rows:], preferred_element_type=jnp.float32)
    outgoing = (next_pack[:tok_rows].astype(jnp.float32) + router_part).astype(jnp.bfloat16)
    return (pre_grad[None], outgoing[None])


def solution(mesh):
    in_specs = (
        P("pipe", "expert", None),
        P("pipe", "expert", None),
        P("pipe", "expert", None),
        P("pipe", "expert", None),
        P("pipe", "expert", None, None),
        P("pipe", "expert", None, None),
        P("pipe", "expert", None),
    )
    out_specs = (P("pipe", "expert", None, None), P("pipe", "expert", None))
    return jax.shard_map(
        per_device, mesh=mesh, in_specs=in_specs, out_specs=out_specs, check_vma=False
    )
```

```python
import jax
import jax.numpy as jnp
from jax import lax
from jax.sharding import PartitionSpec as P


def passed_along(value, axis, by):
    peers = lax.axis_size(axis)
    return lax.ppermute(value, axis, [(i, (i + by) % peers) for i in range(peers)])


def per_device(grad_out, expert_ids, slot_ids, gate_weights, saved_pre, down_weight, router_weight):
    groups = lax.axis_size("expert")
    local_experts = down_weight.shape[1]
    hidden_width = down_weight.shape[2]
    tok_rows = grad_out.shape[1]
    width = grad_out.shape[2]
    top_count = expert_ids.shape[2]
    expert_total = local_experts * groups
    capacity = tok_rows * top_count // expert_total
    total_rows = expert_total * capacity
    chunk = width // capacity
    features = grad_out[0]

    route_ids = expert_ids[0]
    kept_pairs = slot_ids[0] < capacity
    pair_dest = jnp.where(kept_pairs, route_ids * capacity + jnp.minimum(slot_ids[0], capacity - 1), total_rows)
    row_ids = jnp.arange(total_rows, dtype=jnp.int32)
    token_hit = pair_dest[None, :, :] == row_ids[:, None, None]
    token_onehot = jnp.any(token_hit, axis=2).astype(jnp.bfloat16)
    token_rows = jnp.dot(token_onehot, features, preferred_element_type=jnp.float32).astype(jnp.bfloat16)
    matches = token_hit.reshape(total_rows, tok_rows * top_count)
    gate_low = gate_weights[0].astype(jnp.bfloat16)
    slot_gate = jnp.sum(
        jnp.where(matches, gate_low.reshape(-1).astype(jnp.float32)[None, :], jnp.float32(0.0)),
        axis=1,
    )

    gate_cols = jnp.zeros((total_rows, 128), jnp.bfloat16).at[:, 0].set(slot_gate.astype(jnp.bfloat16))
    router_chunks = jnp.broadcast_to(
        router_weight[0].reshape(1, local_experts * capacity, chunk),
        (groups, local_experts * capacity, chunk),
    ).reshape(total_rows, chunk)
    payload = jnp.concatenate([token_rows, router_chunks, gate_cols], axis=1)
    arrived = lax.all_to_all(
        payload.reshape(groups, local_experts * capacity, -1),
        "expert",
        split_axis=0,
        concat_axis=0,
        tiled=True,
    )
    gate_in = arrived[..., width + chunk].reshape(groups, local_experts, capacity).astype(jnp.float32)
    router_full = arrived[..., width : width + chunk].reshape(expert_total, width)
    rows_in = arrived[..., :width].reshape(groups, local_experts, capacity, width).astype(jnp.float32)

    pre_saved = saved_pre[0]
    gate_part = pre_saved[..., :hidden_width].astype(jnp.float32)
    up_part = pre_saved[..., hidden_width:].astype(jnp.float32)
    sigmoid_gate = jax.nn.sigmoid(gate_part)
    silu_gate = gate_part * sigmoid_gate
    hidden = (silu_gate * up_part).astype(jnp.bfloat16)
    weights = down_weight[0]
    expert_out = jnp.einsum(
        "jsf,jfd->jsd", hidden, weights, preferred_element_type=jnp.float32
    ).astype(jnp.bfloat16)
    expert_out = lax.optimization_barrier(expert_out).reshape(local_experts, groups, capacity, width)
    row_scores = jnp.sum(
        rows_in * expert_out.transpose(1, 0, 2, 3).astype(jnp.float32), axis=-1
    )
    returned = lax.all_to_all(
        row_scores.reshape(groups, local_experts * capacity),
        "expert",
        split_axis=0,
        concat_axis=0,
        tiled=True,
    )
    pair_scores = jnp.sum(
        jnp.where(matches, returned.reshape(total_rows)[:, None], jnp.float32(0.0)), axis=0
    ).reshape(tok_rows, top_count)

    scaled_rows = (gate_in[..., None] * rows_in).astype(jnp.bfloat16)
    row_grad = jnp.einsum(
        "gjsd,jfd->jgsf", scaled_rows, weights, preferred_element_type=jnp.float32
    ).reshape(local_experts, groups * capacity, hidden_width)
    gate_grad = row_grad * up_part * sigmoid_gate * (1.0 + gate_part * (1.0 - sigmoid_gate))
    up_grad = row_grad * silu_gate
    pre_grad = jnp.concatenate([gate_grad, up_grad], axis=-1).astype(jnp.bfloat16)

    gate_values = gate_weights[0]
    weighted_sum = jnp.sum(gate_values * pair_scores, axis=-1, keepdims=True)
    select_grad = gate_values * (pair_scores - weighted_sum)
    expert_columns = jnp.arange(expert_total, dtype=jnp.int32)
    chosen = route_ids[:, :, None] == expert_columns[None, None, :]
    logit_grad = jnp.sum(
        jnp.where(chosen, select_grad[:, :, None], jnp.float32(0.0)), axis=1
    ).astype(jnp.bfloat16)
    router_part = jnp.dot(logit_grad, router_full, preferred_element_type=jnp.float32)
    section_grad = (features.astype(jnp.float32) + router_part).astype(jnp.bfloat16)
    outgoing = passed_along(section_grad, "pipe", -1)
    return (pre_grad[None], outgoing[None])


def solution(mesh):
    in_specs = (
        P("pipe", "expert", None),
        P("pipe", "expert", None),
        P("pipe", "expert", None),
        P("pipe", "expert", None),
        P("pipe", "expert", None, None),
        P("pipe", "expert", None, None),
        P("pipe", "expert", None),
    )
    out_specs = (P("pipe", "expert", None, None), P("pipe", "expert", None))
    return jax.shard_map(
        per_device, mesh=mesh, in_specs=in_specs, out_specs=out_specs, check_vma=False
    )
```

```python
import jax
import jax.numpy as jnp
from jax import lax
from jax.sharding import PartitionSpec as P


def passed_along(value, axis, by):
    peers = lax.axis_size(axis)
    return lax.ppermute(value, axis, [(i, (i + by) % peers) for i in range(peers)])


def section_step(grad_out, expert_ids, slot_ids, gate_weights, saved_pre, down_weight, router_weight):
    groups = lax.axis_size("expert")
    local_experts = down_weight.shape[1]
    hidden_width = down_weight.shape[2]
    tok_rows = grad_out.shape[1]
    width = grad_out.shape[2]
    top_count = expert_ids.shape[2]
    expert_total = local_experts * groups
    capacity = tok_rows * top_count // expert_total
    total_rows = expert_total * capacity
    chunk = width // capacity
    features = grad_out[0]

    route_ids = expert_ids[0]
    kept_pairs = slot_ids[0] < capacity
    pair_dest = jnp.where(kept_pairs, route_ids * capacity + jnp.minimum(slot_ids[0], capacity - 1), total_rows)
    row_ids = jnp.arange(total_rows, dtype=jnp.int32)
    token_hit = pair_dest[None, :, :] == row_ids[:, None, None]
    token_onehot = jnp.any(token_hit, axis=2).astype(jnp.bfloat16)
    token_rows = jnp.dot(token_onehot, features, preferred_element_type=jnp.float32).astype(jnp.bfloat16)
    matches = token_hit.reshape(total_rows, tok_rows * top_count)
    gate_low = gate_weights[0].astype(jnp.bfloat16)
    slot_gate = jnp.sum(
        jnp.where(matches, gate_low.reshape(-1).astype(jnp.float32)[None, :], jnp.float32(0.0)),
        axis=1,
    )

    gate_cols = jnp.zeros((total_rows, 128), jnp.bfloat16).at[:, 0].set(slot_gate.astype(jnp.bfloat16))
    router_chunks = jnp.broadcast_to(
        router_weight[0].reshape(1, local_experts * capacity, chunk),
        (groups, local_experts * capacity, chunk),
    ).reshape(total_rows, chunk)
    payload = jnp.concatenate([token_rows, router_chunks, gate_cols], axis=1)
    arrived = lax.all_to_all(
        payload.reshape(groups, local_experts * capacity, -1),
        "expert",
        split_axis=0,
        concat_axis=0,
        tiled=True,
    )
    gate_in = arrived[..., width + chunk].reshape(groups, local_experts, capacity).astype(jnp.float32)
    router_full = arrived[..., width : width + chunk].reshape(expert_total, width)
    rows_in = arrived[..., :width].reshape(groups, local_experts, capacity, width).astype(jnp.float32)

    next_pack = passed_along(jnp.concatenate([features, router_full], axis=0), "pipe", -1)

    pre_saved = saved_pre[0]
    gate_part = pre_saved[..., :hidden_width].astype(jnp.float32)
    up_part = pre_saved[..., hidden_width:].astype(jnp.float32)
    sigmoid_gate = jax.nn.sigmoid(gate_part)
    silu_gate = gate_part * sigmoid_gate
    hidden = (silu_gate * up_part).astype(jnp.bfloat16)
    weights = down_weight[0]
    expert_out = jnp.einsum(
        "jsf,jfd->jsd", hidden, weights, preferred_element_type=jnp.float32
    ).astype(jnp.bfloat16)
    expert_out = lax.optimization_barrier(expert_out).reshape(local_experts, groups, capacity, width)
    row_scores = jnp.sum(
        rows_in * expert_out.transpose(1, 0, 2, 3).astype(jnp.float32), axis=-1
    )
    returned = lax.all_to_all(
        row_scores.reshape(groups, local_experts * capacity),
        "expert",
        split_axis=0,
        concat_axis=0,
        tiled=True,
    )
    pair_scores = jnp.sum(
        jnp.where(matches, returned.reshape(total_rows)[:, None], jnp.float32(0.0)), axis=0
    ).reshape(tok_rows, top_count)

    scaled_rows = (gate_in[..., None] * rows_in).astype(jnp.bfloat16)
    row_grad = jnp.einsum(
        "gjsd,jfd->jgsf", scaled_rows, weights, preferred_element_type=jnp.float32
    ).reshape(local_experts, groups * capacity, hidden_width)
    gate_grad = row_grad * up_part * sigmoid_gate * (1.0 + gate_part * (1.0 - sigmoid_gate))
    up_grad = row_grad * silu_gate
    pre_grad = jnp.concatenate([gate_grad, up_grad], axis=-1).astype(jnp.bfloat16)

    gate_values = gate_weights[0]
    weighted_sum = jnp.sum(gate_values * pair_scores, axis=-1, keepdims=True)
    select_grad = gate_values * (pair_scores - weighted_sum)
    expert_columns = jnp.arange(expert_total, dtype=jnp.int32)
    chosen = route_ids[:, :, None] == expert_columns[None, None, :]
    logit_grad = jnp.sum(
        jnp.where(chosen, select_grad[:, :, None], jnp.float32(0.0)), axis=1
    ).astype(jnp.bfloat16)
    next_logit_grad = passed_along(logit_grad, "pipe", -1)
    router_part = jnp.dot(next_logit_grad, next_pack[tok_rows:], preferred_element_type=jnp.float32)
    outgoing = (next_pack[:tok_rows].astype(jnp.float32) + router_part).astype(jnp.bfloat16)
    return (pre_grad[None], outgoing[None])


def solution(mesh):
    in_specs = (
        P("pipe", "expert", None),
        P("pipe", "expert", None),
        P("pipe", "expert", None),
        P("pipe", "expert", None),
        P("pipe", "expert", None, None),
        P("pipe", "expert", None, None),
        P("pipe", "expert", None),
    )
    out_specs = (P("pipe", "expert", None, None), P("pipe", "expert", None))
    return jax.shard_map(section_step, mesh=mesh, in_specs=in_specs, out_specs=out_specs, check_vma=False)
```

```python
import jax
import jax.numpy as jnp
from jax import lax
from jax.sharding import PartitionSpec as P


def passed_along(value, axis, by):
    peers = lax.axis_size(axis)
    return lax.ppermute(value, axis, [(i, (i + by) % peers) for i in range(peers)])


def section_step(grad_out, expert_ids, slot_ids, gate_weights, saved_pre, down_weight, router_weight):
    groups = lax.axis_size("expert")
    local_experts = down_weight.shape[1]
    hidden_width = down_weight.shape[2]
    tok_rows = grad_out.shape[1]
    width = grad_out.shape[2]
    top_count = expert_ids.shape[2]
    expert_total = local_experts * groups
    capacity = tok_rows * top_count // expert_total
    total_rows = expert_total * capacity
    chunk = width // capacity
    features = grad_out[0]

    route_ids = expert_ids[0]
    kept_pairs = slot_ids[0] < capacity
    pair_dest = jnp.where(kept_pairs, route_ids * capacity + jnp.minimum(slot_ids[0], capacity - 1), total_rows)
    row_ids = jnp.arange(total_rows, dtype=jnp.int32)
    token_hit = pair_dest[None, :, :] == row_ids[:, None, None]
    token_onehot = jnp.any(token_hit, axis=2).astype(jnp.bfloat16)
    token_rows = jnp.dot(token_onehot, features, preferred_element_type=jnp.float32).astype(jnp.bfloat16)
    matches = token_hit.reshape(total_rows, tok_rows * top_count)
    gate_low = gate_weights[0].astype(jnp.bfloat16)
    slot_gate = jnp.sum(
        jnp.where(matches, gate_low.reshape(-1).astype(jnp.float32)[None, :], jnp.float32(0.0)),
        axis=1,
    )

    gate_cols = jnp.zeros((total_rows, 128), jnp.bfloat16).at[:, 0].set(slot_gate.astype(jnp.bfloat16))
    next_router = passed_along(router_weight[0], "pipe", -1)
    router_chunks = jnp.broadcast_to(
        next_router.reshape(1, local_experts * capacity, chunk),
        (groups, local_experts * capacity, chunk),
    ).reshape(total_rows, chunk)
    payload = jnp.concatenate([token_rows, router_chunks, gate_cols], axis=1)
    arrived = lax.all_to_all(
        payload.reshape(groups, local_experts * capacity, -1),
        "expert",
        split_axis=0,
        concat_axis=0,
        tiled=True,
    )
    gate_in = arrived[..., width + chunk].reshape(groups, local_experts, capacity).astype(jnp.float32)
    router_full = arrived[..., width : width + chunk].reshape(expert_total, width)
    rows_in = arrived[..., :width].reshape(groups, local_experts, capacity, width).astype(jnp.float32)

    held, router_full = lax.optimization_barrier((features, router_full))
    next_features = passed_along(held, "pipe", -1)

    pre_saved = saved_pre[0]
    gate_part = pre_saved[..., :hidden_width].astype(jnp.float32)
    up_part = pre_saved[..., hidden_width:].astype(jnp.float32)
    sigmoid_gate = jax.nn.sigmoid(gate_part)
    silu_gate = gate_part * sigmoid_gate
    hidden = (silu_gate * up_part).astype(jnp.bfloat16)
    weights = down_weight[0]
    expert_out = jnp.einsum(
        "jsf,jfd->jsd", hidden, weights, preferred_element_type=jnp.float32
    ).astype(jnp.bfloat16)
    expert_out = lax.optimization_barrier(expert_out).reshape(local_experts, groups, capacity, width)
    row_scores = jnp.sum(
        rows_in * expert_out.transpose(1, 0, 2, 3).astype(jnp.float32), axis=-1
    )
    returned = lax.all_to_all(
        row_scores.reshape(groups, local_experts * capacity),
        "expert",
        split_axis=0,
        concat_axis=0,
        tiled=True,
    )
    pair_scores = jnp.sum(
        jnp.where(matches, returned.reshape(total_rows)[:, None], jnp.float32(0.0)), axis=0
    ).reshape(tok_rows, top_count)

    scaled_rows = (gate_in[..., None] * rows_in).astype(jnp.bfloat16)
    row_grad = jnp.einsum(
        "gjsd,jfd->jgsf", scaled_rows, weights, preferred_element_type=jnp.float32
    ).reshape(local_experts, groups * capacity, hidden_width)
    gate_grad = row_grad * up_part * sigmoid_gate * (1.0 + gate_part * (1.0 - sigmoid_gate))
    up_grad = row_grad * silu_gate
    pre_grad = jnp.concatenate([gate_grad, up_grad], axis=-1).astype(jnp.bfloat16)

    gate_values = gate_weights[0]
    weighted_sum = jnp.sum(gate_values * pair_scores, axis=-1, keepdims=True)
    select_grad = gate_values * (pair_scores - weighted_sum)
    expert_columns = jnp.arange(expert_total, dtype=jnp.int32)
    chosen = route_ids[:, :, None] == expert_columns[None, None, :]
    logit_grad = jnp.sum(
        jnp.where(chosen, select_grad[:, :, None], jnp.float32(0.0)), axis=1
    ).astype(jnp.bfloat16)
    next_logit_grad = passed_along(logit_grad, "pipe", -1)
    router_part = jnp.dot(next_logit_grad, router_full, preferred_element_type=jnp.float32)
    outgoing = (next_features.astype(jnp.float32) + router_part).astype(jnp.bfloat16)
    return (pre_grad[None], outgoing[None])


def solution(mesh):
    in_specs = (
        P("pipe", "expert", None),
        P("pipe", "expert", None),
        P("pipe", "expert", None),
        P("pipe", "expert", None),
        P("pipe", "expert", None, None),
        P("pipe", "expert", None, None),
        P("pipe", "expert", None),
    )
    out_specs = (P("pipe", "expert", None, None), P("pipe", "expert", None))
    return jax.shard_map(section_step, mesh=mesh, in_specs=in_specs, out_specs=out_specs, check_vma=False)
```

```python
import jax
import jax.numpy as jnp
from jax import lax
from jax.sharding import PartitionSpec as P


def passed_along(value, axis, by):
    peers = lax.axis_size(axis)
    return lax.ppermute(value, axis, [(i, (i + by) % peers) for i in range(peers)])


def section_step(grad_out, expert_ids, slot_ids, gate_weights, saved_pre, down_weight, router_weight):
    groups = lax.axis_size("expert")
    local_experts = down_weight.shape[1]
    hidden_width = down_weight.shape[2]
    tok_rows = grad_out.shape[1]
    width = grad_out.shape[2]
    top_count = expert_ids.shape[2]
    expert_total = local_experts * groups
    capacity = tok_rows * top_count // expert_total
    total_rows = expert_total * capacity
    chunk = width // capacity
    features = grad_out[0]

    route_ids = expert_ids[0]
    kept_pairs = slot_ids[0] < capacity
    pair_dest = jnp.where(kept_pairs, route_ids * capacity + jnp.minimum(slot_ids[0], capacity - 1), total_rows)
    row_ids = jnp.arange(total_rows, dtype=jnp.int32)
    token_hit = pair_dest[None, :, :] == row_ids[:, None, None]
    token_onehot = jnp.any(token_hit, axis=2).astype(jnp.bfloat16)
    matches = token_hit.reshape(total_rows, tok_rows * top_count)
    gate_low = gate_weights[0].astype(jnp.bfloat16)
    slot_gate = jnp.sum(
        jnp.where(matches, gate_low.reshape(-1).astype(jnp.float32)[None, :], jnp.float32(0.0)),
        axis=1,
    )

    gate_cols = jnp.zeros((total_rows, 128), jnp.bfloat16).at[:, 0].set(slot_gate.astype(jnp.bfloat16))
    next_router = passed_along(router_weight[0], "pipe", -1)
    router_chunks = jnp.broadcast_to(
        next_router.reshape(1, local_experts * capacity, chunk),
        (groups, local_experts * capacity, chunk),
    ).reshape(total_rows, chunk)
    wide_features = jnp.concatenate([features, jnp.zeros((tok_rows, chunk + 128), features.dtype)], axis=1)
    extras = jnp.concatenate(
        [jnp.zeros((total_rows, width), jnp.float32), router_chunks.astype(jnp.float32), gate_cols.astype(jnp.float32)],
        axis=1,
    )
    payload = (
        jnp.dot(token_onehot, wide_features, preferred_element_type=jnp.float32) + extras
    ).astype(jnp.bfloat16)
    arrived = lax.all_to_all(
        payload.reshape(groups, local_experts * capacity, -1),
        "expert",
        split_axis=0,
        concat_axis=0,
        tiled=True,
    )
    gate_in = arrived[..., width + chunk].reshape(groups, local_experts, capacity).astype(jnp.float32)
    router_full = arrived[..., width : width + chunk].reshape(expert_total, width)
    rows_in = arrived[..., :width].reshape(groups, local_experts, capacity, width).astype(jnp.float32)

    held, router_full = lax.optimization_barrier((features, router_full))
    next_features = passed_along(held, "pipe", -1)

    pre_saved = saved_pre[0]
    gate_part = pre_saved[..., :hidden_width].astype(jnp.float32)
    up_part = pre_saved[..., hidden_width:].astype(jnp.float32)
    sigmoid_gate = jax.nn.sigmoid(gate_part)
    silu_gate = gate_part * sigmoid_gate
    hidden = (silu_gate * up_part).astype(jnp.bfloat16)
    weights = down_weight[0]
    expert_out = jnp.einsum(
        "jsf,jfd->jsd", hidden, weights, preferred_element_type=jnp.float32
    ).astype(jnp.bfloat16)
    expert_out = lax.optimization_barrier(expert_out).reshape(local_experts, groups, capacity, width)
    row_scores = jnp.sum(
        rows_in * expert_out.transpose(1, 0, 2, 3).astype(jnp.float32), axis=-1
    )
    returned = lax.all_to_all(
        row_scores.reshape(groups, local_experts * capacity),
        "expert",
        split_axis=0,
        concat_axis=0,
        tiled=True,
    )
    pair_scores = jnp.sum(
        jnp.where(matches, returned.reshape(total_rows)[:, None], jnp.float32(0.0)), axis=0
    ).reshape(tok_rows, top_count)

    scaled_rows = (gate_in[..., None] * rows_in).astype(jnp.bfloat16)
    row_grad = jnp.einsum(
        "gjsd,jfd->jgsf", scaled_rows, weights, preferred_element_type=jnp.float32
    ).reshape(local_experts, groups * capacity, hidden_width)
    gate_grad = row_grad * up_part * sigmoid_gate * (1.0 + gate_part * (1.0 - sigmoid_gate))
    up_grad = row_grad * silu_gate
    pre_grad = jnp.concatenate([gate_grad, up_grad], axis=-1).astype(jnp.bfloat16)

    gate_values = gate_weights[0]
    weighted_sum = jnp.sum(gate_values * pair_scores, axis=-1, keepdims=True)
    select_grad = gate_values * (pair_scores - weighted_sum)
    expert_columns = jnp.arange(expert_total, dtype=jnp.int32)
    chosen = route_ids[:, :, None] == expert_columns[None, None, :]
    logit_grad = jnp.sum(
        jnp.where(chosen, select_grad[:, :, None], jnp.float32(0.0)), axis=1
    ).astype(jnp.bfloat16)
    next_logit_grad = passed_along(logit_grad, "pipe", -1)
    router_part = jnp.dot(next_logit_grad, router_full, preferred_element_type=jnp.float32)
    outgoing = (next_features.astype(jnp.float32) + router_part).astype(jnp.bfloat16)
    return (pre_grad[None], outgoing[None])


def solution(mesh):
    in_specs = (
        P("pipe", "expert", None),
        P("pipe", "expert", None),
        P("pipe", "expert", None),
        P("pipe", "expert", None),
        P("pipe", "expert", None, None),
        P("pipe", "expert", None, None),
        P("pipe", "expert", None),
    )
    out_specs = (P("pipe", "expert", None, None), P("pipe", "expert", None))
    return jax.shard_map(section_step, mesh=mesh, in_specs=in_specs, out_specs=out_specs, check_vma=False)
```

```python
import jax
import jax.numpy as jnp
from jax import lax
from jax.sharding import PartitionSpec as P


def passed_along(value, axis, by):
    peers = lax.axis_size(axis)
    return lax.ppermute(value, axis, [(i, (i + by) % peers) for i in range(peers)])


def section_step(grad_out, expert_ids, slot_ids, gate_weights, saved_pre, down_weight, router_weight):
    groups = lax.axis_size("expert")
    local_experts = down_weight.shape[1]
    hidden_width = down_weight.shape[2]
    tok_rows = grad_out.shape[1]
    width = grad_out.shape[2]
    top_count = expert_ids.shape[2]
    expert_total = local_experts * groups
    capacity = tok_rows * top_count // expert_total
    total_rows = expert_total * capacity
    chunk = width // capacity
    features = grad_out[0]

    route_ids = expert_ids[0]
    kept_pairs = slot_ids[0] < capacity
    pair_dest = jnp.where(kept_pairs, route_ids * capacity + jnp.minimum(slot_ids[0], capacity - 1), total_rows)
    row_ids = jnp.arange(total_rows, dtype=jnp.int32)
    token_hit = pair_dest[None, :, :] == row_ids[:, None, None]
    token_onehot = jnp.any(token_hit, axis=2).astype(jnp.bfloat16)
    matches = token_hit.reshape(total_rows, tok_rows * top_count)
    gate_low = gate_weights[0].astype(jnp.bfloat16)
    slot_gate = jnp.sum(
        jnp.where(matches, gate_low.reshape(-1).astype(jnp.float32)[None, :], jnp.float32(0.0)),
        axis=1,
    )

    gate_cols = jnp.zeros((total_rows, 128), jnp.bfloat16).at[:, 0].set(slot_gate.astype(jnp.bfloat16))
    next_router = passed_along(router_weight[0], "pipe", -1)
    router_chunks = jnp.broadcast_to(
        next_router.reshape(1, local_experts * capacity, chunk),
        (groups, local_experts * capacity, chunk),
    ).reshape(total_rows, chunk)
    wide_features = jnp.concatenate([features, jnp.zeros((tok_rows, chunk + 128), features.dtype)], axis=1)
    extras = jnp.concatenate(
        [jnp.zeros((total_rows, width), jnp.float32), router_chunks.astype(jnp.float32), gate_cols.astype(jnp.float32)],
        axis=1,
    )
    payload = (
        jnp.dot(token_onehot, wide_features, preferred_element_type=jnp.float32) + extras
    ).astype(jnp.bfloat16)
    arrived = lax.all_to_all(
        payload.reshape(groups, local_experts * capacity, -1),
        "expert",
        split_axis=0,
        concat_axis=0,
        tiled=True,
    )
    gate_in = arrived[..., width + chunk].reshape(groups, local_experts, capacity).astype(jnp.float32)
    router_full = arrived[..., width : width + chunk].reshape(expert_total, width)
    wide = arrived.shape[-1]
    rows_in = arrived.reshape(groups, local_experts, capacity, wide).astype(jnp.float32)

    held, router_full = lax.optimization_barrier((features, router_full))
    next_features = passed_along(held, "pipe", -1)

    pre_saved = saved_pre[0]
    gate_part = pre_saved[..., :hidden_width].astype(jnp.float32)
    up_part = pre_saved[..., hidden_width:].astype(jnp.float32)
    sigmoid_gate = jax.nn.sigmoid(gate_part)
    silu_gate = gate_part * sigmoid_gate
    hidden = (silu_gate * up_part).astype(jnp.bfloat16)
    weights = down_weight[0]
    expert_out = jnp.einsum(
        "jsf,jfd->jsd", hidden, weights, preferred_element_type=jnp.float32
    ).astype(jnp.bfloat16)
    expert_out = jnp.pad(lax.optimization_barrier(expert_out), ((0, 0), (0, 0), (0, wide - width)))
    expert_out = expert_out.reshape(local_experts, groups, capacity, wide)
    wide_weights = jnp.pad(weights, ((0, 0), (0, 0), (0, wide - width)))
    row_scores = jnp.sum(
        rows_in * expert_out.transpose(1, 0, 2, 3).astype(jnp.float32), axis=-1
    )
    returned = lax.all_to_all(
        row_scores.reshape(groups, local_experts * capacity),
        "expert",
        split_axis=0,
        concat_axis=0,
        tiled=True,
    )
    pair_scores = jnp.sum(
        jnp.where(matches, returned.reshape(total_rows)[:, None], jnp.float32(0.0)), axis=0
    ).reshape(tok_rows, top_count)

    scaled_rows = (gate_in[..., None] * rows_in).astype(jnp.bfloat16)
    row_grad = jnp.einsum(
        "gjsd,jfd->jgsf", scaled_rows, wide_weights, preferred_element_type=jnp.float32
    ).reshape(local_experts, groups * capacity, hidden_width)
    gate_grad = row_grad * up_part * sigmoid_gate * (1.0 + gate_part * (1.0 - sigmoid_gate))
    up_grad = row_grad * silu_gate
    pre_grad = jnp.concatenate([gate_grad, up_grad], axis=-1).astype(jnp.bfloat16)

    gate_values = gate_weights[0]
    weighted_sum = jnp.sum(gate_values * pair_scores, axis=-1, keepdims=True)
    select_grad = gate_values * (pair_scores - weighted_sum)
    expert_columns = jnp.arange(expert_total, dtype=jnp.int32)
    chosen = route_ids[:, :, None] == expert_columns[None, None, :]
    logit_grad = jnp.sum(
        jnp.where(chosen, select_grad[:, :, None], jnp.float32(0.0)), axis=1
    ).astype(jnp.bfloat16)
    next_logit_grad = passed_along(logit_grad, "pipe", -1)
    router_part = jnp.dot(next_logit_grad, router_full, preferred_element_type=jnp.float32)
    outgoing = (next_features.astype(jnp.float32) + router_part).astype(jnp.bfloat16)
    return (pre_grad[None], outgoing[None])


def solution(mesh):
    in_specs = (
        P("pipe", "expert", None),
        P("pipe", "expert", None),
        P("pipe", "expert", None),
        P("pipe", "expert", None),
        P("pipe", "expert", None, None),
        P("pipe", "expert", None, None),
        P("pipe", "expert", None),
    )
    out_specs = (P("pipe", "expert", None, None), P("pipe", "expert", None))
    return jax.shard_map(section_step, mesh=mesh, in_specs=in_specs, out_specs=out_specs, check_vma=False)
```

```python
import jax
import jax.numpy as jnp
from jax import lax
from jax.sharding import PartitionSpec as P


def passed_along(value, axis, by):
    peers = lax.axis_size(axis)
    return lax.ppermute(value, axis, [(i, (i + by) % peers) for i in range(peers)])


def section_step(grad_out, expert_ids, slot_ids, gate_weights, saved_pre, down_weight, router_weight):
    groups = lax.axis_size("expert")
    local_experts = down_weight.shape[1]
    hidden_width = down_weight.shape[2]
    tok_rows = grad_out.shape[1]
    width = grad_out.shape[2]
    top_count = expert_ids.shape[2]
    expert_total = local_experts * groups
    capacity = tok_rows * top_count // expert_total
    total_rows = expert_total * capacity
    chunk = width // capacity
    features = grad_out[0]

    route_ids = expert_ids[0]
    kept_pairs = slot_ids[0] < capacity
    pair_dest = jnp.where(kept_pairs, route_ids * capacity + jnp.minimum(slot_ids[0], capacity - 1), total_rows)
    row_ids = jnp.arange(total_rows, dtype=jnp.int32)
    token_hit = pair_dest[None, :, :] == row_ids[:, None, None]
    token_onehot = jnp.any(token_hit, axis=2).astype(jnp.bfloat16)
    matches = token_hit.reshape(total_rows, tok_rows * top_count)
    gate_low = gate_weights[0].astype(jnp.bfloat16)
    slot_gate = jnp.sum(
        jnp.where(matches, gate_low.reshape(-1).astype(jnp.float32)[None, :], jnp.float32(0.0)),
        axis=1,
    )

    gate_cols = jnp.zeros((total_rows, 128), jnp.bfloat16).at[:, 0].set(slot_gate.astype(jnp.bfloat16))
    next_router = passed_along(router_weight[0], "pipe", -1)
    router_chunks = jnp.broadcast_to(
        next_router.reshape(1, local_experts * capacity, chunk),
        (groups, local_experts * capacity, chunk),
    ).reshape(total_rows, chunk)
    wide_features = jnp.concatenate([features, jnp.zeros((tok_rows, chunk + 128), features.dtype)], axis=1)
    extras = jnp.concatenate(
        [jnp.zeros((total_rows, width), jnp.float32), router_chunks.astype(jnp.float32), gate_cols.astype(jnp.float32)],
        axis=1,
    )
    payload = (
        jnp.dot(token_onehot, wide_features, preferred_element_type=jnp.float32) + extras
    ).astype(jnp.bfloat16)
    arrived = lax.all_to_all(
        payload.reshape(groups, local_experts * capacity, -1),
        "expert",
        split_axis=0,
        concat_axis=0,
        tiled=True,
    )
    gate_in = arrived[..., width + chunk].reshape(groups, local_experts, capacity).astype(jnp.float32)
    router_full = arrived[..., width : width + chunk].reshape(expert_total, width)
    wide = arrived.shape[-1]
    rows_in = arrived.reshape(groups, local_experts, capacity, wide).astype(jnp.float32)

    held, router_full = lax.optimization_barrier((features, router_full))
    next_features = passed_along(held, "pipe", -1)

    pre_saved = saved_pre[0]
    gate_part = pre_saved[..., :hidden_width].astype(jnp.float32)
    up_part = pre_saved[..., hidden_width:].astype(jnp.float32)
    sigmoid_gate = jax.nn.sigmoid(gate_part)
    silu_gate = gate_part * sigmoid_gate
    hidden = (silu_gate * up_part).astype(jnp.bfloat16)
    weights = down_weight[0]
    expert_out = jnp.einsum(
        "jsf,jfd->jsd", hidden, weights, preferred_element_type=jnp.float32
    ).astype(jnp.bfloat16)
    expert_out = jnp.pad(expert_out, ((0, 0), (0, 0), (0, wide - width)))
    expert_out = lax.optimization_barrier(
        expert_out.reshape(local_experts, groups, capacity, wide).transpose(1, 0, 2, 3)
    )
    wide_weights = jnp.pad(weights, ((0, 0), (0, 0), (0, wide - width)))
    row_scores = jnp.sum(
        rows_in * expert_out.astype(jnp.float32), axis=-1
    )
    returned = lax.all_to_all(
        row_scores.reshape(groups, local_experts * capacity),
        "expert",
        split_axis=0,
        concat_axis=0,
        tiled=True,
    )
    pair_scores = jnp.sum(
        jnp.where(matches, returned.reshape(total_rows)[:, None], jnp.float32(0.0)), axis=0
    ).reshape(tok_rows, top_count)

    scaled_rows = (gate_in[..., None] * rows_in).astype(jnp.bfloat16)
    row_grad = jnp.einsum(
        "gjsd,jfd->jgsf", scaled_rows, wide_weights, preferred_element_type=jnp.float32
    ).reshape(local_experts, groups * capacity, hidden_width)
    gate_grad = row_grad * up_part * sigmoid_gate * (1.0 + gate_part * (1.0 - sigmoid_gate))
    up_grad = row_grad * silu_gate
    pre_grad = jnp.concatenate([gate_grad, up_grad], axis=-1).astype(jnp.bfloat16)

    gate_values = gate_weights[0]
    weighted_sum = jnp.sum(gate_values * pair_scores, axis=-1, keepdims=True)
    select_grad = gate_values * (pair_scores - weighted_sum)
    expert_columns = jnp.arange(expert_total, dtype=jnp.int32)
    chosen = route_ids[:, :, None] == expert_columns[None, None, :]
    logit_grad = jnp.sum(
        jnp.where(chosen, select_grad[:, :, None], jnp.float32(0.0)), axis=1
    ).astype(jnp.bfloat16)
    next_logit_grad = passed_along(logit_grad, "pipe", -1)
    router_part = jnp.dot(next_logit_grad, router_full, preferred_element_type=jnp.float32)
    outgoing = (next_features.astype(jnp.float32) + router_part).astype(jnp.bfloat16)
    return (pre_grad[None], outgoing[None])


def solution(mesh):
    in_specs = (
        P("pipe", "expert", None),
        P("pipe", "expert", None),
        P("pipe", "expert", None),
        P("pipe", "expert", None),
        P("pipe", "expert", None, None),
        P("pipe", "expert", None, None),
        P("pipe", "expert", None),
    )
    out_specs = (P("pipe", "expert", None, None), P("pipe", "expert", None))
    return jax.shard_map(section_step, mesh=mesh, in_specs=in_specs, out_specs=out_specs, check_vma=False)
```
